256 devices in a mesh: lat: 16 (over x_hi, y, core), lon: 16 (over z, x_lo).
Axes of the slice: x: 4 (x_hi: 2, x_lo: 2; x = x_hi * 2 + x_lo), y: 4, z: 8, core: 2. Of those that a mesh axis runs over, the one named last changes fastest.
Arguments:
- initial: float32 [64, 256, 2048], P(None, 'lat', 'lon'), may hold values from -6 to 6
- east_wind: float32 [64, 256, 2048], P(None, 'lat', 'lon'), may hold values from -2.5 to 2.5
- north_wind: float32 [64, 256, 2048], P(None, 'lat', 'lon'), may hold values from -2.5 to 2.5
- east_mask: int32 [64, 256, 2048], P(None, 'lat', 'lon'), may hold values from 0 to 1
- north_mask: int32 [64, 256, 2048], P(None, 'lat', 'lon'), may hold values from 0 to 1
- mixing: float32 [63], replicated, may hold values from 0.02 to 0.2
- obs_cell: int32 [16, 16, 4, 256], P('lat', 'lon'), may hold values from 0 to 2047
- obs_level: int32 [16, 16, 4, 256], P('lat', 'lon'), may hold values from 0 to 63
- obs_value: float32 [16, 16, 4, 256], P('lat', 'lon'), may hold values from -6 to 6
- obs_weight: float32 [16, 16, 4, 256], P('lat', 'lon'), may hold values from 0.2 to 2
Outputs:
- gradient: float32 [64, 256, 2048], P(None, 'lat', 'lon')
- cost: float32 [], replicated
The draws below stay inside these ranges and needn't reach their ends.
Inputs may be any that keep to these rules, and one draw needn't show every extreme that they name: `obs_cell`: row times 128 plus column within the block.
All inputs are finite; a program needn't handle non-finite values.
Results may differ from the reference program's by a relative error of at most 0.0003.
Values sent between devices are 32-bit elements; how exact they have to be, the bound alone decides.
No kernel may reach another device: no remote copies, remote signals or barrier semaphores. Data moves between devices by JAX's collectives and lax.ppermute only.
A program may use at most 64 MiB of HBM per device.

```python
import math
import jax
import jax.numpy as jnp

L = 64
CLAT = 16
CLON = 128
STEPS = 4
NOBS = 256
NY = 256
NX = 2048
N_LAT = 16
N_LON = 16


def with_ends(entries, own_key, least, high):
    longest = entries.shape.index(max(entries.shape))
    spots = []
    for shift in (0, 1):
        where = [jax.random.randint(jax.random.fold_in(own_key, axis), (), 0, length) for axis, length in enumerate(entries.shape)]
        where[longest] = (where[longest] + shift) % entries.shape[longest]
        spots.append(tuple(where))
    return entries.at[spots[0]].set(least).at[spots[1]].set(high)


def shard_levels(stream_key, extent, shards, least, high):
    level = 1.0
    for dim, shards_of in shards:
        draws = jax.random.uniform(jax.random.fold_in(jax.random.fold_in(stream_key, 6), dim), (shards_of,), jnp.float32, least / len(shards), high / len(shards))
        level = level * jnp.repeat(jnp.exp(draws), extent[dim] // shards_of).reshape((-1,) + (1,) * (len(extent) - 1 - dim))
    return level


def normal_values(rng, shape, deviation, limit, shards=(), held_as=jnp.bfloat16):
    values = deviation * jax.random.normal(rng, shape, jnp.float32)
    if shards:
        values = values * shard_levels(rng, shape, shards, -0.22, 0.18)
    return jnp.clip(values, -limit, limit).astype(held_as)


def setup_inputs(seed: int = 0) -> dict:
    keys = jax.random.split(jax.random.key(seed), 11)
    return {
        "initial": normal_values(keys[0], (L, NY, NX), 1.0, 6.0, ((1, 16), (2, 16)), jnp.float32),
        "east_wind": normal_values(keys[1], (L, NY, NX), 0.2, 2.5, ((1, 16), (2, 16)), jnp.float32),
        "north_wind": normal_values(keys[2], (L, NY, NX), 0.2, 2.5, ((1, 16), (2, 16)), jnp.float32),
        "east_mask": with_ends(jax.random.randint(keys[3], (L, NY, NX), 0, 2), jax.random.fold_in(keys[3], 1), 0, 1).astype(jnp.int32),
        "north_mask": with_ends(jax.random.randint(keys[4], (L, NY, NX), 0, 2), jax.random.fold_in(keys[4], 1), 0, 1).astype(jnp.int32),
        "mixing": jnp.clip(jnp.exp(jax.random.uniform(keys[5], (L - 1,), jnp.float32, math.log(0.02), math.log(0.2))), 0.02, 0.2),
        "obs_cell": with_ends(jax.random.randint(keys[6], (N_LAT, N_LON, STEPS, NOBS), 0, CLAT * CLON), jax.random.fold_in(keys[6], 1), 0, (CLAT * CLON) - 1).astype(jnp.int32),
        "obs_level": with_ends(jax.random.randint(keys[7], (N_LAT, N_LON, STEPS, NOBS), 0, L), jax.random.fold_in(keys[7], 1), 0, L - 1).astype(jnp.int32),
        "obs_value": normal_values(keys[8], (N_LAT, N_LON, STEPS, NOBS), 1.0, 6.0, ((0, 16), (1, 16)), jnp.float32),
        "obs_weight": jnp.clip(jnp.exp(math.log(2.0) - 2.3025851 * jax.random.uniform(keys[9], (N_LAT, N_LON, STEPS, NOBS), jnp.float32) ** shard_levels(keys[9], (N_LAT, N_LON, STEPS, NOBS), ((0, 16), (1, 16)), -0.2, 0.2)), 0.2, 2.0),
    }


def face_parts(velocity, branch):
    share = jnp.where(branch == 1, jnp.where(velocity > 0, 1.0, 0.0), 0.5)
    return (velocity * share, velocity * (1.0 - share))

def vertical(field, mixing):
    flux = mixing[:, None, None] * (field[1:] - field[:-1])
    zero_row = jnp.zeros_like(field[:1])
    return jnp.concatenate([flux, zero_row], 0) - jnp.concatenate([zero_row, flux], 0)

def reference(initial, east_wind, north_wind, east_mask, north_mask, mixing, obs_cell, obs_level, obs_value, obs_weight):
    west_p, west_q = face_parts(east_wind, east_mask)
    south_p, south_q = face_parts(north_wind, north_mask)
    keep = (jnp.arange(NY) > 0)[None, :, None]
    south_p = jnp.where(keep, south_p, 0.0)
    south_q = jnp.where(keep, south_q, 0.0)
    east_p = jnp.roll(west_p, -1, 2)
    east_q = jnp.roll(west_q, -1, 2)
    zero_line = jnp.zeros_like(south_p[:, :1])
    north_p = jnp.concatenate([south_p[:, 1:], zero_line], 1)
    north_q = jnp.concatenate([south_q[:, 1:], zero_line], 1)

    def advance(field):
        west = jnp.roll(field, 1, 2)
        east = jnp.roll(field, -1, 2)
        blank = jnp.zeros_like(field[:, :1])
        south = jnp.concatenate([blank, field[:, :-1]], 1)
        north = jnp.concatenate([field[:, 1:], blank], 1)
        div_lon = east_p * field + east_q * east - west_p * west - west_q * field
        div_lat = north_p * field + north_q * north - south_p * south - south_q * field
        return field + vertical(field, mixing) - div_lon - div_lat
    flat = (obs_level * (CLAT * CLON) + obs_cell).astype(jnp.int32)
    lat_ids = jnp.arange(N_LAT)[:, None, None]
    lon_ids = jnp.arange(N_LON)[None, :, None]

    def misfit(start):
        state = start
        total = jnp.zeros((), jnp.float32)
        for step in range(STEPS):
            state = advance(state)
            blocks = state.reshape(L, N_LAT, CLAT, N_LON, CLON).transpose(1, 3, 0, 2, 4).reshape(N_LAT, N_LON, L * CLAT * CLON)
            picked = blocks[lat_ids, lon_ids, flat[:, :, step]]
            innovation = picked - obs_value[:, :, step]
            total = total + 0.5 * jnp.sum(obs_weight[:, :, step] * innovation * innovation)
        return total
    cost, pull = jax.vjp(misfit, initial)
    gradient = pull(jnp.ones_like(cost))[0]
    return (gradient, cost)
```

```python
import jax
import jax.numpy as jnp
from jax import lax
from jax.sharding import PartitionSpec as P

STEPS = 4
HALO = 2 * STEPS


def face_parts(velocity, branch):
    share = jnp.where(branch == 1, jnp.where(velocity > 0, 1.0, 0.0), 0.5)
    return (velocity * share, velocity * (1.0 - share))


def vertical(field, mixing):
    flux = mixing[:, None, None] * (field[1:] - field[:-1])
    zero_row = jnp.zeros_like(field[:1])
    return jnp.concatenate([flux, zero_row], 0) - jnp.concatenate([zero_row, flux], 0)


def swap(block, axis, width, dim, periodic, extra):
    count = lax.axis_size(axis)
    forward = [(i, i + 1) for i in range(count - 1)]
    if periodic:
        forward.append((count - 1, 0))
    backward = [(t, s) for s, t in forward]
    size = block.shape[dim]
    hi = lax.slice_in_dim(block, size - width, size, axis=dim)
    lo = lax.slice_in_dim(block, 0, width, axis=dim)
    n = hi.size
    low = lax.ppermute(jnp.concatenate([hi.reshape(-1), extra]), axis, forward)
    high = lax.ppermute(jnp.concatenate([lo.reshape(-1), extra]), axis, backward)
    shape = hi.shape
    grown = jnp.concatenate([low[:n].reshape(shape), block, high[:n].reshape(shape)], axis=dim)
    return grown, low[n:], high[n:]


def on_device(
    initial,
    east_wind,
    north_wind,
    east_mask,
    north_mask,
    mixing,
    obs_cell,
    obs_level,
    obs_value,
    obs_weight,
):
    levels, rows, cols = initial.shape
    h = HALO
    west_p, west_q = face_parts(east_wind, east_mask)
    south_p, south_q = face_parts(north_wind, north_mask)
    global_row = lax.axis_index("lat") * rows + lax.iota(jnp.int32, rows)
    keep = (global_row > 0)[None, :, None]
    south_p = jnp.where(keep, south_p, 0.0)
    south_q = jnp.where(keep, south_q, 0.0)

    fields = jnp.stack([initial, west_p, west_q, south_p, south_q])
    obs = jnp.stack(
        [
            obs_cell[0, 0].astype(jnp.float32),
            obs_level[0, 0].astype(jnp.float32),
            obs_value[0, 0],
            obs_weight[0, 0],
        ]
    ).reshape(-1)
    fields, obs_w, obs_e = swap(fields, "lon", h, 3, True, obs)
    row_obs = jnp.concatenate([obs_w, obs, obs_e])
    fields, obs_s, obs_n = swap(fields, "lat", h, 2, False, row_obs)

    state = fields[0]
    west_p, west_q, south_p, south_q = fields[1], fields[2], fields[3], fields[4]
    east_p = jnp.roll(west_p, -1, 2)
    east_q = jnp.roll(west_q, -1, 2)
    north_p = jnp.roll(south_p, -1, 1)
    north_q = jnp.roll(south_q, -1, 1)
    ext_rows, ext_cols = rows + 2 * h, cols + 2 * h

    sets = []
    for dr, payload in ((-1, obs_s), (0, row_obs), (1, obs_n)):
        parts = payload.reshape(3, 4, STEPS, -1)
        for j, dc in enumerate((-1, 0, 1)):
            sets.append((dr, dc, parts[j]))
    cells = jnp.stack([p[0] for _, _, p in sets]).astype(jnp.int32)
    lev = jnp.stack([p[1] for _, _, p in sets]).astype(jnp.int32)
    val = jnp.stack([p[2] for _, _, p in sets])
    wgt = jnp.stack([p[3] for _, _, p in sets])
    dr = jnp.array([s[0] for s in sets], jnp.int32)[:, None, None]
    dc = jnp.array([s[1] for s in sets], jnp.int32)[:, None, None]
    own = jnp.array([s[0] == 0 and s[1] == 0 for s in sets])[:, None, None]
    er = dr * rows + cells // cols + h
    ec = dc * cols + cells % cols + h

    def forward_step(field):
        west = jnp.roll(field, 1, 2)
        east = jnp.roll(field, -1, 2)
        south = jnp.roll(field, 1, 1)
        north = jnp.roll(field, -1, 1)
        div_lon = east_p * field + east_q * east - west_p * west - west_q * field
        div_lat = north_p * field + north_q * north - south_p * south - south_q * field
        return field + vertical(field, mixing) - div_lon - div_lat

    def reverse_step(adjoint):
        west = jnp.roll(adjoint, 1, 2)
        east = jnp.roll(adjoint, -1, 2)
        south = jnp.roll(adjoint, 1, 1)
        north = jnp.roll(adjoint, -1, 1)
        back_lon = -(east_p - west_q) * adjoint - west_q * west + east_p * east
        back_lat = -(north_p - south_q) * adjoint - south_q * south + north_p * north
        return adjoint + vertical(adjoint, mixing) + back_lon + back_lat

    local_cost = jnp.zeros((), jnp.float32)
    injections = []
    for step in range(STEPS):
        state = forward_step(state)
        k = step + 1
        valid = (er[:, step] >= k) & (er[:, step] < ext_rows - k)
        valid = valid & (ec[:, step] >= k) & (ec[:, step] < ext_cols - k)
        li = jnp.where(valid, lev[:, step], 0)
        ri = jnp.where(valid, er[:, step], 0)
        ci = jnp.where(valid, ec[:, step], 0)
        picked = state[li, ri, ci]
        innovation = picked - val[:, step]
        weighted = jnp.where(valid, wgt[:, step] * innovation, 0.0)
        mine = own[:, 0]
        local_cost = local_cost + 0.5 * jnp.sum(jnp.where(mine, weighted * innovation, 0.0))
        injections.append(
            jnp.zeros((levels, ext_rows, ext_cols), jnp.float32).at[li, ri, ci].add(weighted)
        )
    adjoint = jnp.zeros((levels, ext_rows, ext_cols), jnp.float32)
    for step in range(STEPS - 1, -1, -1):
        adjoint = reverse_step(adjoint + injections[step])
    gradient = adjoint[:, h : h + rows, h : h + cols]
    cost = lax.psum(local_cost, ("lat", "lon"))
    return (gradient, cost)


def solution(mesh):
    placed = (
        P(None, "lat", "lon"),
        P(None, "lat", "lon"),
        P(None, "lat", "lon"),
        P(None, "lat", "lon"),
        P(None, "lat", "lon"),
        P(),
        P("lat", "lon", None, None),
        P("lat", "lon", None, None),
        P("lat", "lon", None, None),
        P("lat", "lon", None, None),
    )
    return jax.shard_map(
        on_device,
        mesh=mesh,
        in_specs=placed,
        out_specs=(P(None, "lat", "lon"), P()),
        check_vma=False,
    )
```

```python
import jax
import jax.numpy as jnp
from jax import lax
from jax.sharding import PartitionSpec as P

STEPS = 4
HALO = STEPS


def face_parts(velocity, branch):
    share = jnp.where(branch == 1, jnp.where(velocity > 0, 1.0, 0.0), 0.5)
    return (velocity * share, velocity * (1.0 - share))


def vertical(field, mixing):
    flux = mixing[:, None, None] * (field[1:] - field[:-1])
    zero_row = jnp.zeros_like(field[:1])
    return jnp.concatenate([flux, zero_row], 0) - jnp.concatenate([zero_row, flux], 0)


def ring(axis, periodic):
    count = lax.axis_size(axis)
    up = [(i, i + 1) for i in range(count - 1)]
    if periodic:
        up.append((count - 1, 0))
    down = [(t, s) for s, t in up]
    return up, down


def grow(block, axis, width, dim, periodic):
    up, down = ring(axis, periodic)
    size = block.shape[dim]
    low = lax.ppermute(lax.slice_in_dim(block, size - width, size, axis=dim), axis, up)
    high = lax.ppermute(lax.slice_in_dim(block, 0, width, axis=dim), axis, down)
    return jnp.concatenate([low, block, high], axis=dim)


def fold(block, axis, width, dim, periodic):
    up, down = ring(axis, periodic)
    size = block.shape[dim]
    from_high = lax.ppermute(lax.slice_in_dim(block, size - width, size, axis=dim), axis, up)
    from_low = lax.ppermute(lax.slice_in_dim(block, 0, width, axis=dim), axis, down)
    inner = lax.slice_in_dim(block, width, size - width, axis=dim)
    n = inner.shape[dim]
    pad_lo = [(0, 0)] * block.ndim
    pad_hi = [(0, 0)] * block.ndim
    pad_lo[dim] = (0, n - width)
    pad_hi[dim] = (n - width, 0)
    return inner + jnp.pad(from_high, pad_lo) + jnp.pad(from_low, pad_hi)


def on_device(
    initial,
    east_wind,
    north_wind,
    east_mask,
    north_mask,
    mixing,
    obs_cell,
    obs_level,
    obs_value,
    obs_weight,
):
    levels, rows, cols = initial.shape
    h = HALO
    west_p, west_q = face_parts(east_wind, east_mask)
    south_p, south_q = face_parts(north_wind, north_mask)
    global_row = lax.axis_index("lat") * rows + lax.iota(jnp.int32, rows)
    keep = (global_row > 0)[None, :, None]
    south_p = jnp.where(keep, south_p, 0.0)
    south_q = jnp.where(keep, south_q, 0.0)

    fields = jnp.stack([initial, west_p, west_q, south_p, south_q])
    fields = grow(fields, "lon", h, 3, True)
    fields = grow(fields, "lat", h, 2, False)

    state = fields[0]
    px, qx, py, qy = fields[1], fields[2], fields[3], fields[4]
    pxe = jnp.roll(px, -1, 2)
    qxe = jnp.roll(qx, -1, 2)
    pyn = jnp.roll(py, -1, 1)
    qyn = jnp.roll(qy, -1, 1)
    centre = (pxe - qx) + (pyn - qy)

    def forward_step(x):
        west = jnp.roll(x, 1, 2)
        east = jnp.roll(x, -1, 2)
        south = jnp.roll(x, 1, 1)
        north = jnp.roll(x, -1, 1)
        flow = centre * x + qxe * east - px * west + qyn * north - py * south
        return x + vertical(x, mixing) - flow

    def reverse_step(a):
        west = jnp.roll(a, 1, 2)
        east = jnp.roll(a, -1, 2)
        south = jnp.roll(a, 1, 1)
        north = jnp.roll(a, -1, 1)
        back = -centre * a - qx * west + pxe * east - qy * south + pyn * north
        return a + vertical(a, mixing) + back

    flat = obs_level[0, 0] * (rows * cols) + obs_cell[0, 0]
    local_cost = jnp.zeros((), jnp.float32)
    injections = []
    for step in range(STEPS):
        state = forward_step(state)
        inner = state[:, h : h + rows, h : h + cols]
        innovation = inner.reshape(-1)[flat[step]] - obs_value[0, 0, step]
        weighted = obs_weight[0, 0, step] * innovation
        local_cost = local_cost + 0.5 * jnp.sum(weighted * innovation)
        injected = jnp.zeros((levels * rows * cols,), jnp.float32).at[flat[step]].add(weighted)
        injections.append(jnp.pad(injected.reshape(levels, rows, cols), ((0, 0), (h, h), (h, h))))
    adjoint = jnp.zeros_like(injections[0])
    for step in range(STEPS - 1, -1, -1):
        adjoint = reverse_step(adjoint + injections[step])
    adjoint = fold(adjoint, "lat", h, 1, False)
    gradient = fold(adjoint, "lon", h, 2, True)
    cost = lax.psum(local_cost, ("lat", "lon"))
    return (gradient, cost)


def solution(mesh):
    placed = (
        P(None, "lat", "lon"),
        P(None, "lat", "lon"),
        P(None, "lat", "lon"),
        P(None, "lat", "lon"),
        P(None, "lat", "lon"),
        P(),
        P("lat", "lon", None, None),
        P("lat", "lon", None, None),
        P("lat", "lon", None, None),
        P("lat", "lon", None, None),
    )
    return jax.shard_map(
        on_device,
        mesh=mesh,
        in_specs=placed,
        out_specs=(P(None, "lat", "lon"), P()),
        check_vma=False,
    )
```

```python
import jax
import jax.numpy as jnp
from jax import lax
from jax.sharding import PartitionSpec as P

STEPS = 4
HALO = STEPS


def face_parts(velocity, branch):
    share = jnp.where(branch == 1, jnp.where(velocity > 0, 1.0, 0.0), 0.5)
    return (velocity * share, velocity * (1.0 - share))


def vertical(field, mixing):
    flux = mixing[:, None, None] * (field[1:] - field[:-1])
    zero_row = jnp.zeros_like(field[:1])
    return jnp.concatenate([flux, zero_row], 0) - jnp.concatenate([zero_row, flux], 0)


def ring(axis, periodic):
    count = lax.axis_size(axis)
    up = [(i, i + 1) for i in range(count - 1)]
    if periodic:
        up.append((count - 1, 0))
    down = [(t, s) for s, t in up]
    return up, down


def grow(block, axis, width, dim, periodic):
    up, down = ring(axis, periodic)
    size = block.shape[dim]
    low = lax.ppermute(lax.slice_in_dim(block, size - width, size, axis=dim), axis, up)
    high = lax.ppermute(lax.slice_in_dim(block, 0, width, axis=dim), axis, down)
    return jnp.concatenate([low, block, high], axis=dim)


def fold(block, axis, width, dim, periodic):
    up, down = ring(axis, periodic)
    size = block.shape[dim]
    from_high = lax.ppermute(lax.slice_in_dim(block, size - width, size, axis=dim), axis, up)
    from_low = lax.ppermute(lax.slice_in_dim(block, 0, width, axis=dim), axis, down)
    inner = lax.slice_in_dim(block, width, size - width, axis=dim)
    n = inner.shape[dim]
    pad_lo = [(0, 0)] * block.ndim
    pad_hi = [(0, 0)] * block.ndim
    pad_lo[dim] = (0, n - width)
    pad_hi[dim] = (n - width, 0)
    return inner + jnp.pad(from_high, pad_lo) + jnp.pad(from_low, pad_hi)


def total(value, axes):
    for axis in axes:
        count = lax.axis_size(axis)
        step = 1
        while step < count:
            pairs = [(i, i ^ step) for i in range(count)]
            value = value + lax.ppermute(value, axis, pairs)
            step *= 2
    return value


def on_device(
    initial,
    east_wind,
    north_wind,
    east_mask,
    north_mask,
    mixing,
    obs_cell,
    obs_level,
    obs_value,
    obs_weight,
):
    levels, rows, cols = initial.shape
    h = HALO
    west_p, west_q = face_parts(east_wind, east_mask)
    south_p, south_q = face_parts(north_wind, north_mask)
    global_row = lax.axis_index("lat") * rows + lax.iota(jnp.int32, rows)
    keep = (global_row > 0)[None, :, None]
    south_p = jnp.where(keep, south_p, 0.0)
    south_q = jnp.where(keep, south_q, 0.0)

    fields = jnp.stack([initial, west_p, west_q, south_p, south_q])
    fields = grow(fields, "lon", h, 3, True)
    fields = grow(fields, "lat", h, 2, False)

    state = fields[0]
    px, qx, py, qy = fields[1], fields[2], fields[3], fields[4]
    pxe = jnp.roll(px, -1, 2)
    qxe = jnp.roll(qx, -1, 2)
    pyn = jnp.roll(py, -1, 1)
    qyn = jnp.roll(qy, -1, 1)
    centre = (pxe - qx) + (pyn - qy)

    def forward_step(x):
        west = jnp.roll(x, 1, 2)
        east = jnp.roll(x, -1, 2)
        south = jnp.roll(x, 1, 1)
        north = jnp.roll(x, -1, 1)
        flow = centre * x + qxe * east - px * west + qyn * north - py * south
        return x + vertical(x, mixing) - flow

    def reverse_step(a):
        west = jnp.roll(a, 1, 2)
        east = jnp.roll(a, -1, 2)
        south = jnp.roll(a, 1, 1)
        north = jnp.roll(a, -1, 1)
        back = -centre * a - qx * west + pxe * east - qy * south + pyn * north
        return a + vertical(a, mixing) + back

    flat = obs_level[0, 0] * (rows * cols) + obs_cell[0, 0]
    local_cost = jnp.zeros((), jnp.float32)
    injections = []
    for step in range(STEPS):
        state = forward_step(state)
        inner = state[:, h : h + rows, h : h + cols]
        innovation = inner.reshape(-1)[flat[step]] - obs_value[0, 0, step]
        weighted = obs_weight[0, 0, step] * innovation
        local_cost = local_cost + 0.5 * jnp.sum(weighted * innovation)
        injected = jnp.zeros((levels * rows * cols,), jnp.float32).at[flat[step]].add(weighted)
        injections.append(jnp.pad(injected.reshape(levels, rows, cols), ((0, 0), (h, h), (h, h))))
    adjoint = jnp.zeros_like(injections[0])
    for step in range(STEPS - 1, -1, -1):
        adjoint = reverse_step(adjoint + injections[step])
    adjoint = fold(adjoint, "lat", h, 1, False)
    gradient = fold(adjoint, "lon", h, 2, True)
    cost = total(local_cost, ("lon", "lat"))
    return (gradient, cost)


def solution(mesh):
    placed = (
        P(None, "lat", "lon"),
        P(None, "lat", "lon"),
        P(None, "lat", "lon"),
        P(None, "lat", "lon"),
        P(None, "lat", "lon"),
        P(),
        P("lat", "lon", None, None),
        P("lat", "lon", None, None),
        P("lat", "lon", None, None),
        P("lat", "lon", None, None),
    )
    return jax.shard_map(
        on_device,
        mesh=mesh,
        in_specs=placed,
        out_specs=(P(None, "lat", "lon"), P()),
        check_vma=False,
    )
```

```python
import jax
import jax.numpy as jnp
from jax import lax
from jax.sharding import PartitionSpec as P

STEPS = 4
HALO = STEPS


def face_parts(velocity, branch):
    share = jnp.where(branch == 1, jnp.where(velocity > 0, 1.0, 0.0), 0.5)
    return (velocity * share, velocity * (1.0 - share))


def vertical(field, mixing):
    flux = mixing[:, None, None] * (field[1:] - field[:-1])
    zero_row = jnp.zeros_like(field[:1])
    return jnp.concatenate([flux, zero_row], 0) - jnp.concatenate([zero_row, flux], 0)


def ring(axis, periodic):
    count = lax.axis_size(axis)
    up = [(i, i + 1) for i in range(count - 1)]
    if periodic:
        up.append((count - 1, 0))
    down = [(t, s) for s, t in up]
    return up, down


def grow(block, axis, width, dim, periodic):
    up, down = ring(axis, periodic)
    size = block.shape[dim]
    low = lax.ppermute(lax.slice_in_dim(block, size - width, size, axis=dim), axis, up)
    high = lax.ppermute(lax.slice_in_dim(block, 0, width, axis=dim), axis, down)
    return jnp.concatenate([low, block, high], axis=dim)


def fold(block, axis, width, dim, periodic):
    up, down = ring(axis, periodic)
    size = block.shape[dim]
    from_high = lax.ppermute(lax.slice_in_dim(block, size - width, size, axis=dim), axis, up)
    from_low = lax.ppermute(lax.slice_in_dim(block, 0, width, axis=dim), axis, down)
    inner = lax.slice_in_dim(block, width, size - width, axis=dim)
    n = inner.shape[dim]
    pad_lo = [(0, 0)] * block.ndim
    pad_hi = [(0, 0)] * block.ndim
    pad_lo[dim] = (0, n - width)
    pad_hi[dim] = (n - width, 0)
    return inner + jnp.pad(from_high, pad_lo) + jnp.pad(from_low, pad_hi)


def combine(value, axis, stride):
    index = lax.axis_index(axis)
    count = lax.axis_size(axis)
    got = [value]
    for d in (1, 2, 3):
        pairs = [(i, i ^ (d * stride)) for i in range(count)]
        got.append(lax.ppermute(value, axis, pairs))
    got = jnp.stack(got)
    pos = (index // stride) % 4
    ordered = got[pos ^ jnp.arange(4)]
    return (ordered[0] + ordered[1]) + (ordered[2] + ordered[3])


def rounds(axes):
    plan = []
    for axis in axes:
        stride = 1
        while stride < lax.axis_size(axis):
            plan.append((axis, stride))
            stride *= 4
    return plan


def on_device(
    initial,
    east_wind,
    north_wind,
    east_mask,
    north_mask,
    mixing,
    obs_cell,
    obs_level,
    obs_value,
    obs_weight,
):
    levels, rows, cols = initial.shape
    h = HALO
    west_p, west_q = face_parts(east_wind, east_mask)
    south_p, south_q = face_parts(north_wind, north_mask)
    global_row = lax.axis_index("lat") * rows + lax.iota(jnp.int32, rows)
    keep = (global_row > 0)[None, :, None]
    south_p = jnp.where(keep, south_p, 0.0)
    south_q = jnp.where(keep, south_q, 0.0)

    fields = jnp.stack([initial, west_p, west_q, south_p, south_q])
    fields = grow(fields, "lon", h, 3, True)
    fields = grow(fields, "lat", h, 2, False)

    state = fields[0]
    px, qx, py, qy = fields[1], fields[2], fields[3], fields[4]
    pxe = jnp.roll(px, -1, 2)
    qxe = jnp.roll(qx, -1, 2)
    pyn = jnp.roll(py, -1, 1)
    qyn = jnp.roll(qy, -1, 1)
    centre = (pxe - qx) + (pyn - qy)

    def forward_step(x):
        west = jnp.roll(x, 1, 2)
        east = jnp.roll(x, -1, 2)
        south = jnp.roll(x, 1, 1)
        north = jnp.roll(x, -1, 1)
        flow = centre * x + qxe * east - px * west + qyn * north - py * south
        return x + vertical(x, mixing) - flow

    def reverse_step(a):
        west = jnp.roll(a, 1, 2)
        east = jnp.roll(a, -1, 2)
        south = jnp.roll(a, 1, 1)
        north = jnp.roll(a, -1, 1)
        back = -centre * a - qx * west + pxe * east - qy * south + pyn * north
        return a + vertical(a, mixing) + back

    flat = obs_level[0, 0] * (rows * cols) + obs_cell[0, 0]
    local_cost = jnp.zeros((), jnp.float32)
    injections = []
    for step in range(STEPS):
        state = forward_step(state)
        inner = state[:, h : h + rows, h : h + cols]
        innovation = inner.reshape(-1)[flat[step]] - obs_value[0, 0, step]
        weighted = obs_weight[0, 0, step] * innovation
        local_cost = local_cost + 0.5 * jnp.sum(weighted * innovation)
        injected = jnp.zeros((levels * rows * cols,), jnp.float32).at[flat[step]].add(weighted)
        injections.append(jnp.pad(injected.reshape(levels, rows, cols), ((0, 0), (h, h), (h, h))))
    adjoint = jnp.zeros_like(injections[0])
    plan = rounds(("lon", "lat"))
    value = local_cost
    for j, step in enumerate(range(STEPS - 1, -1, -1)):
        adjoint = reverse_step(adjoint + injections[step])
        if j < len(plan):
            value = combine(value, *plan[j])
            value, adjoint = lax.optimization_barrier((value, adjoint))
    for axis, stride in plan[STEPS:]:
        value = combine(value, axis, stride)
    adjoint = fold(adjoint, "lat", h, 1, False)
    gradient = fold(adjoint, "lon", h, 2, True)
    cost = value
    return (gradient, cost)


def solution(mesh):
    placed = (
        P(None, "lat", "lon"),
        P(None, "lat", "lon"),
        P(None, "lat", "lon"),
        P(None, "lat", "lon"),
        P(None, "lat", "lon"),
        P(),
        P("lat", "lon", None, None),
        P("lat", "lon", None, None),
        P("lat", "lon", None, None),
        P("lat", "lon", None, None),
    )
    return jax.shard_map(
        on_device,
        mesh=mesh,
        in_specs=placed,
        out_specs=(P(None, "lat", "lon"), P()),
        check_vma=False,
    )
```

```python
import jax
import jax.numpy as jnp
from jax import lax
from jax.sharding import PartitionSpec as P

STEPS = 4
HALO = STEPS


def face_parts(velocity, branch):
    share = jnp.where(branch == 1, jnp.where(velocity > 0, 1.0, 0.0), 0.5)
    return (velocity * share, velocity * (1.0 - share))


def vertical(field, mixing):
    flux = mixing[:, None, None] * (field[1:] - field[:-1])
    zero_row = jnp.zeros_like(field[:1])
    return jnp.concatenate([flux, zero_row], 0) - jnp.concatenate([zero_row, flux], 0)


def ring(axis, periodic):
    count = lax.axis_size(axis)
    up = [(i, i + 1) for i in range(count - 1)]
    if periodic:
        up.append((count - 1, 0))
    down = [(t, s) for s, t in up]
    return up, down


def grow(block, axis, width, dim, periodic):
    up, down = ring(axis, periodic)
    size = block.shape[dim]
    low = lax.ppermute(lax.slice_in_dim(block, size - width, size, axis=dim), axis, up)
    high = lax.ppermute(lax.slice_in_dim(block, 0, width, axis=dim), axis, down)
    return jnp.concatenate([low, block, high], axis=dim)


def fold(block, axis, width, dim, periodic):
    up, down = ring(axis, periodic)
    size = block.shape[dim]
    from_high = lax.ppermute(lax.slice_in_dim(block, size - width, size, axis=dim), axis, up)
    from_low = lax.ppermute(lax.slice_in_dim(block, 0, width, axis=dim), axis, down)
    inner = lax.slice_in_dim(block, width, size - width, axis=dim)
    n = inner.shape[dim]
    pad_lo = [(0, 0)] * block.ndim
    pad_hi = [(0, 0)] * block.ndim
    pad_lo[dim] = (0, n - width)
    pad_hi[dim] = (n - width, 0)
    return inner + jnp.pad(from_high, pad_lo) + jnp.pad(from_low, pad_hi)


def total(value, axes):
    for axis in axes:
        count = lax.axis_size(axis)
        step = 1
        while step < count:
            pairs = [(i, i ^ step) for i in range(count)]
            value = value + lax.ppermute(value, axis, pairs)
            step *= 2
    return value


def on_device(
    initial,
    east_wind,
    north_wind,
    east_mask,
    north_mask,
    mixing,
    obs_cell,
    obs_level,
    obs_value,
    obs_weight,
):
    levels, rows, cols = initial.shape
    h = HALO
    west_p, west_q = face_parts(east_wind, east_mask)
    south_p, south_q = face_parts(north_wind, north_mask)
    global_row = lax.axis_index("lat") * rows + lax.iota(jnp.int32, rows)
    keep = (global_row > 0)[None, :, None]
    south_p = jnp.where(keep, south_p, 0.0)
    south_q = jnp.where(keep, south_q, 0.0)

    fields = jnp.stack([initial, west_p, west_q, south_p, south_q])
    fields = grow(fields, "lon", h, 3, True)
    fields = grow(fields, "lat", h, 2, False)

    state = fields[0]
    px, qx, py, qy = fields[1], fields[2], fields[3], fields[4]
    pxe = jnp.roll(px, -1, 2)
    qxe = jnp.roll(qx, -1, 2)
    pyn = jnp.roll(py, -1, 1)
    qyn = jnp.roll(qy, -1, 1)
    centre = (pxe - qx) + (pyn - qy)

    def forward_step(x):
        west = jnp.roll(x, 1, 2)
        east = jnp.roll(x, -1, 2)
        south = jnp.roll(x, 1, 1)
        north = jnp.roll(x, -1, 1)
        flow = centre * x + qxe * east - px * west + qyn * north - py * south
        return x + vertical(x, mixing) - flow

    def reverse_step(a):
        west = jnp.roll(a, 1, 2)
        east = jnp.roll(a, -1, 2)
        south = jnp.roll(a, 1, 1)
        north = jnp.roll(a, -1, 1)
        back = -centre * a - qx * west + pxe * east - qy * south + pyn * north
        return a + vertical(a, mixing) + back

    flat = obs_level[0, 0] * (rows * cols) + obs_cell[0, 0]
    local_cost = jnp.zeros((), jnp.float32)
    injections = []
    for step in range(STEPS):
        state = forward_step(state)
        inner = state[:, h : h + rows, h : h + cols]
        innovation = inner.reshape(-1)[flat[step]] - obs_value[0, 0, step]
        weighted = obs_weight[0, 0, step] * innovation
        local_cost = local_cost + 0.5 * jnp.sum(weighted * innovation)
        injected = jnp.zeros((levels * rows * cols,), jnp.float32).at[flat[step]].add(weighted)
        injections.append(jnp.pad(injected.reshape(levels, rows, cols), ((0, 0), (h, h), (h, h))))
    adjoint = jnp.zeros_like(injections[0])
    for step in range(STEPS - 1, -1, -1):
        adjoint = reverse_step(adjoint + injections[step])
    adjoint = fold(adjoint, "lat", h, 1, False)
    gradient = fold(adjoint, "lon", h, 2, True)
    spread = jnp.zeros((8, 128), jnp.float32).at[0, 0].set(local_cost)
    every = lax.all_gather(spread, ("lat", "lon"), tiled=True)
    cost = jnp.sum(every[::8, 0])
    return (gradient, cost)


def solution(mesh):
    placed = (
        P(None, "lat", "lon"),
        P(None, "lat", "lon"),
        P(None, "lat", "lon"),
        P(None, "lat", "lon"),
        P(None, "lat", "lon"),
        P(),
        P("lat", "lon", None, None),
        P("lat", "lon", None, None),
        P("lat", "lon", None, None),
        P("lat", "lon", None, None),
    )
    return jax.shard_map(
        on_device,
        mesh=mesh,
        in_specs=placed,
        out_specs=(P(None, "lat", "lon"), P()),
        check_vma=False,
    )
```

```python
import jax
import jax.numpy as jnp
from jax import lax
from jax.sharding import PartitionSpec as P

STEPS = 4
HALO = STEPS


def face_parts(velocity, branch):
    share = jnp.where(branch == 1, jnp.where(velocity > 0, 1.0, 0.0), 0.5)
    return (velocity * share, velocity * (1.0 - share))


def vertical(field, mixing):
    flux = mixing.reshape((-1,) + (1,) * (field.ndim - 1)) * (field[1:] - field[:-1])
    zero_row = jnp.zeros_like(field[:1])
    return jnp.concatenate([flux, zero_row], 0) - jnp.concatenate([zero_row, flux], 0)


def ring(axis, periodic):
    count = lax.axis_size(axis)
    up = [(i, i + 1) for i in range(count - 1)]
    if periodic:
        up.append((count - 1, 0))
    down = [(t, s) for s, t in up]
    return up, down


def grow(block, axis, width, dim, periodic):
    up, down = ring(axis, periodic)
    size = block.shape[dim]
    low = lax.ppermute(lax.slice_in_dim(block, size - width, size, axis=dim), axis, up)
    high = lax.ppermute(lax.slice_in_dim(block, 0, width, axis=dim), axis, down)
    return jnp.concatenate([low, block, high], axis=dim)


def fold(block, axis, width, dim, periodic):
    up, down = ring(axis, periodic)
    size = block.shape[dim]
    from_high = lax.ppermute(lax.slice_in_dim(block, size - width, size, axis=dim), axis, up)
    from_low = lax.ppermute(lax.slice_in_dim(block, 0, width, axis=dim), axis, down)
    inner = lax.slice_in_dim(block, width, size - width, axis=dim)
    n = inner.shape[dim]
    pad_lo = [(0, 0)] * block.ndim
    pad_hi = [(0, 0)] * block.ndim
    pad_lo[dim] = (0, n - width)
    pad_hi[dim] = (n - width, 0)
    return inner + jnp.pad(from_high, pad_lo) + jnp.pad(from_low, pad_hi)


def total(value, axes):
    for axis in axes:
        count = lax.axis_size(axis)
        step = 1
        while step < count:
            pairs = [(i, i ^ step) for i in range(count)]
            value = value + lax.ppermute(value, axis, pairs)
            step *= 2
    return value


def on_device(
    initial,
    east_wind,
    north_wind,
    east_mask,
    north_mask,
    mixing,
    obs_cell,
    obs_level,
    obs_value,
    obs_weight,
):
    levels, rows, cols = initial.shape
    h = HALO
    west_p, west_q = face_parts(east_wind, east_mask)
    south_p, south_q = face_parts(north_wind, north_mask)
    global_row = lax.axis_index("lat") * rows + lax.iota(jnp.int32, rows)
    keep = (global_row > 0)[None, :, None]
    south_p = jnp.where(keep, south_p, 0.0)
    south_q = jnp.where(keep, south_q, 0.0)

    fields = jnp.stack([initial, west_p, west_q, south_p, south_q])
    fields = grow(fields, "lon", h, 3, True)
    fields = grow(fields, "lat", h, 2, False)

    ext_rows, ext_cols = rows + 2 * h, cols + 2 * h
    flat_fields = fields.reshape(5, levels, ext_rows * ext_cols)
    state = flat_fields[0]
    px, qx, py, qy = flat_fields[1], flat_fields[2], flat_fields[3], flat_fields[4]
    pxe = jnp.roll(px, -1, 1)
    qxe = jnp.roll(qx, -1, 1)
    pyn = jnp.roll(py, -ext_cols, 1)
    qyn = jnp.roll(qy, -ext_cols, 1)
    centre = (pxe - qx) + (pyn - qy)

    def neighbours(x):
        return (
            jnp.roll(x, 1, 1),
            jnp.roll(x, -1, 1),
            jnp.roll(x, ext_cols, 1),
            jnp.roll(x, -ext_cols, 1),
        )

    def forward_step(x):
        west, east, south, north = neighbours(x)
        flow = centre * x + qxe * east - px * west + qyn * north - py * south
        return x + vertical(x, mixing) - flow

    def reverse_step(a):
        west, east, south, north = neighbours(a)
        back = -centre * a - qx * west + pxe * east - qy * south + pyn * north
        return a + vertical(a, mixing) + back

    cell = obs_cell[0, 0]
    flat = obs_level[0, 0] * (ext_rows * ext_cols) + (cell // cols + h) * ext_cols + (cell % cols + h)
    local_cost = jnp.zeros((), jnp.float32)
    injections = []
    for step in range(STEPS):
        state = forward_step(state)
        innovation = state.reshape(-1)[flat[step]] - obs_value[0, 0, step]
        weighted = obs_weight[0, 0, step] * innovation
        local_cost = local_cost + 0.5 * jnp.sum(weighted * innovation)
        injected = jnp.zeros((levels * ext_rows * ext_cols,), jnp.float32).at[flat[step]].add(weighted)
        injections.append(injected.reshape(levels, ext_rows * ext_cols))
    adjoint = jnp.zeros_like(injections[0])
    for step in range(STEPS - 1, -1, -1):
        adjoint = reverse_step(adjoint + injections[step])
    adjoint = adjoint.reshape(levels, ext_rows, ext_cols)
    adjoint = fold(adjoint, "lat", h, 1, False)
    gradient = fold(adjoint, "lon", h, 2, True)
    cost = total(local_cost, ("lon", "lat"))
    return (gradient, cost)


def solution(mesh):
    placed = (
        P(None, "lat", "lon"),
        P(None, "lat", "lon"),
        P(None, "lat", "lon"),
        P(None, "lat", "lon"),
        P(None, "lat", "lon"),
        P(),
        P("lat", "lon", None, None),
        P("lat", "lon", None, None),
        P("lat", "lon", None, None),
        P("lat", "lon", None, None),
    )
    return jax.shard_map(
        on_device,
        mesh=mesh,
        in_specs=placed,
        out_specs=(P(None, "lat", "lon"), P()),
        check_vma=False,
    )
```

```python
import jax
import jax.numpy as jnp
from jax import lax
from jax.sharding import PartitionSpec as P

STEPS = 4
HALO = STEPS


def face_parts(velocity, branch):
    share = jnp.where(branch == 1, jnp.where(velocity > 0, 1.0, 0.0), 0.5)
    return (velocity * share, velocity * (1.0 - share))


def vertical(field, mixing):
    flux = mixing[:, None, None] * (field[1:] - field[:-1])
    zero_row = jnp.zeros_like(field[:1])
    return jnp.concatenate([flux, zero_row], 0) - jnp.concatenate([zero_row, flux], 0)


def ring(axis, periodic):
    count = lax.axis_size(axis)
    up = [(i, i + 1) for i in range(count - 1)]
    if periodic:
        up.append((count - 1, 0))
    down = [(t, s) for s, t in up]
    return up, down


def grow(block, axis, width, dim, periodic):
    up, down = ring(axis, periodic)
    size = block.shape[dim]
    low = lax.ppermute(lax.slice_in_dim(block, size - width, size, axis=dim), axis, up)
    high = lax.ppermute(lax.slice_in_dim(block, 0, width, axis=dim), axis, down)
    return jnp.concatenate([low, block, high], axis=dim)


def fold(block, axis, width, dim, periodic):
    up, down = ring(axis, periodic)
    size = block.shape[dim]
    from_high = lax.ppermute(lax.slice_in_dim(block, size - width, size, axis=dim), axis, up)
    from_low = lax.ppermute(lax.slice_in_dim(block, 0, width, axis=dim), axis, down)
    inner = lax.slice_in_dim(block, width, size - width, axis=dim)
    n = inner.shape[dim]
    pad_lo = [(0, 0)] * block.ndim
    pad_hi = [(0, 0)] * block.ndim
    pad_lo[dim] = (0, n - width)
    pad_hi[dim] = (n - width, 0)
    return inner + jnp.pad(from_high, pad_lo) + jnp.pad(from_low, pad_hi)


def total(value, axes):
    for axis in axes:
        count = lax.axis_size(axis)
        step = 1
        while step < count:
            pairs = [(i, i ^ step) for i in range(count)]
            value = value + lax.ppermute(value, axis, pairs)
            step *= 2
    return value


def on_device(
    initial,
    east_wind,
    north_wind,
    east_mask,
    north_mask,
    mixing,
    obs_cell,
    obs_level,
    obs_value,
    obs_weight,
):
    levels, rows, cols = initial.shape
    h = HALO
    west_p, west_q = face_parts(east_wind, east_mask)
    south_p, south_q = face_parts(north_wind, north_mask)
    global_row = lax.axis_index("lat") * rows + lax.iota(jnp.int32, rows)
    keep = (global_row > 0)[None, :, None]
    south_p = jnp.where(keep, south_p, 0.0)
    south_q = jnp.where(keep, south_q, 0.0)

    fields = jnp.stack([initial, west_p, west_q, south_p, south_q])
    fields = grow(fields, "lon", h, 3, True)
    fields = grow(fields, "lat", h, 2, False)

    state = fields[0]
    px, qx, py, qy = fields[1], fields[2], fields[3], fields[4]
    pxe = jnp.roll(px, -1, 2)
    qxe = jnp.roll(qx, -1, 2)
    pyn = jnp.roll(py, -1, 1)
    qyn = jnp.roll(qy, -1, 1)
    centre = (pxe - qx) + (pyn - qy)

    def forward_step(x):
        west = jnp.roll(x, 1, 2)
        east = jnp.roll(x, -1, 2)
        south = jnp.roll(x, 1, 1)
        north = jnp.roll(x, -1, 1)
        flow = centre * x + qxe * east - px * west + qyn * north - py * south
        return x + vertical(x, mixing) - flow

    def reverse_step(a):
        west = jnp.roll(a, 1, 2)
        east = jnp.roll(a, -1, 2)
        south = jnp.roll(a, 1, 1)
        north = jnp.roll(a, -1, 1)
        back = -centre * a - qx * west + pxe * east - qy * south + pyn * north
        return a + vertical(a, mixing) + back

    flat = obs_level[0, 0] * (rows * cols) + obs_cell[0, 0]
    local_cost = jnp.zeros((), jnp.float32)
    injections = []
    for step in range(STEPS):
        state = forward_step(state)
        inner = state[:, h : h + rows, h : h + cols]
        innovation = inner.reshape(-1)[flat[step]] - obs_value[0, 0, step]
        weighted = obs_weight[0, 0, step] * innovation
        local_cost = local_cost + 0.5 * jnp.sum(weighted * innovation)
        injected = jnp.zeros((levels * rows * cols,), jnp.float32).at[flat[step]].add(weighted)
        injections.append(jnp.pad(injected.reshape(levels, rows, cols), ((0, 0), (h, h), (h, h))))
    adjoint = jnp.zeros_like(injections[0])
    for step in range(STEPS - 1, -1, -1):
        adjoint = reverse_step(adjoint + injections[step])
    adjoint = fold(adjoint, "lat", h, 1, False)
    gradient = fold(adjoint, "lon", h, 2, True)
    cost = lax.psum(lax.psum(local_cost, "lon"), "lat")
    return (gradient, cost)


def solution(mesh):
    placed = (
        P(None, "lat", "lon"),
        P(None, "lat", "lon"),
        P(None, "lat", "lon"),
        P(None, "lat", "lon"),
        P(None, "lat", "lon"),
        P(),
        P("lat", "lon", None, None),
        P("lat", "lon", None, None),
        P("lat", "lon", None, None),
        P("lat", "lon", None, None),
    )
    return jax.shard_map(
        on_device,
        mesh=mesh,
        in_specs=placed,
        out_specs=(P(None, "lat", "lon"), P()),
        check_vma=False,
    )
```

```python
import jax
import jax.numpy as jnp
from jax import lax
from jax.sharding import PartitionSpec as P

STEPS = 4
HALO = STEPS


def face_parts(velocity, branch):
    share = jnp.where(branch == 1, jnp.where(velocity > 0, 1.0, 0.0), 0.5)
    return (velocity * share, velocity * (1.0 - share))


def vertical(field, mixing):
    flux = mixing[:, None, None] * (field[1:] - field[:-1])
    zero_row = jnp.zeros_like(field[:1])
    return jnp.concatenate([flux, zero_row], 0) - jnp.concatenate([zero_row, flux], 0)


def shift(x, offset, dim):
    pad = [(0, 0)] * x.ndim
    size = x.shape[dim]
    if offset > 0:
        pad[dim] = (offset, 0)
        return lax.slice_in_dim(jnp.pad(x, pad), 0, size, axis=dim)
    pad[dim] = (0, -offset)
    return lax.slice_in_dim(jnp.pad(x, pad), -offset, size - offset, axis=dim)


def ring(axis, periodic):
    count = lax.axis_size(axis)
    up = [(i, i + 1) for i in range(count - 1)]
    if periodic:
        up.append((count - 1, 0))
    down = [(t, s) for s, t in up]
    return up, down


def grow(block, axis, width, dim, periodic):
    up, down = ring(axis, periodic)
    size = block.shape[dim]
    low = lax.ppermute(lax.slice_in_dim(block, size - width, size, axis=dim), axis, up)
    high = lax.ppermute(lax.slice_in_dim(block, 0, width, axis=dim), axis, down)
    return jnp.concatenate([low, block, high], axis=dim)


def fold(block, axis, width, dim, periodic):
    up, down = ring(axis, periodic)
    size = block.shape[dim]
    from_high = lax.ppermute(lax.slice_in_dim(block, size - width, size, axis=dim), axis, up)
    from_low = lax.ppermute(lax.slice_in_dim(block, 0, width, axis=dim), axis, down)
    inner = lax.slice_in_dim(block, width, size - width, axis=dim)
    n = inner.shape[dim]
    pad_lo = [(0, 0)] * block.ndim
    pad_hi = [(0, 0)] * block.ndim
    pad_lo[dim] = (0, n - width)
    pad_hi[dim] = (n - width, 0)
    return inner + jnp.pad(from_high, pad_lo) + jnp.pad(from_low, pad_hi)


def total(value, axes):
    for axis in axes:
        count = lax.axis_size(axis)
        step = 1
        while step < count:
            pairs = [(i, i ^ step) for i in range(count)]
            value = value + lax.ppermute(value, axis, pairs)
            step *= 2
    return value


def on_device(
    initial,
    east_wind,
    north_wind,
    east_mask,
    north_mask,
    mixing,
    obs_cell,
    obs_level,
    obs_value,
    obs_weight,
):
    levels, rows, cols = initial.shape
    h = HALO
    west_p, west_q = face_parts(east_wind, east_mask)
    south_p, south_q = face_parts(north_wind, north_mask)
    global_row = lax.axis_index("lat") * rows + lax.iota(jnp.int32, rows)
    keep = (global_row > 0)[None, :, None]
    south_p = jnp.where(keep, south_p, 0.0)
    south_q = jnp.where(keep, south_q, 0.0)

    fields = jnp.stack([initial, west_p, west_q, south_p, south_q])
    fields = grow(fields, "lon", h, 3, True)
    fields = grow(fields, "lat", h, 2, False)

    state = fields[0]
    px, qx, py, qy = fields[1], fields[2], fields[3], fields[4]
    pxe = shift(px, -1, 2)
    qxe = shift(qx, -1, 2)
    pyn = shift(py, -1, 1)
    qyn = shift(qy, -1, 1)
    centre = (pxe - qx) + (pyn - qy)

    def forward_step(x):
        west = shift(x, 1, 2)
        east = shift(x, -1, 2)
        south = shift(x, 1, 1)
        north = shift(x, -1, 1)
        flow = centre * x + qxe * east - px * west + qyn * north - py * south
        return x + vertical(x, mixing) - flow

    def reverse_step(a):
        west = shift(a, 1, 2)
        east = shift(a, -1, 2)
        south = shift(a, 1, 1)
        north = shift(a, -1, 1)
        back = -centre * a - qx * west + pxe * east - qy * south + pyn * north
        return a + vertical(a, mixing) + back

    flat = obs_level[0, 0] * (rows * cols) + obs_cell[0, 0]
    local_cost = jnp.zeros((), jnp.float32)
    injections = []
    for step in range(STEPS):
        state = forward_step(state)
        inner = state[:, h : h + rows, h : h + cols]
        innovation = inner.reshape(-1)[flat[step]] - obs_value[0, 0, step]
        weighted = obs_weight[0, 0, step] * innovation
        local_cost = local_cost + 0.5 * jnp.sum(weighted * innovation)
        injected = jnp.zeros((levels * rows * cols,), jnp.float32).at[flat[step]].add(weighted)
        injections.append(jnp.pad(injected.reshape(levels, rows, cols), ((0, 0), (h, h), (h, h))))
    adjoint = jnp.zeros_like(injections[0])
    for step in range(STEPS - 1, -1, -1):
        adjoint = reverse_step(adjoint + injections[step])
    adjoint = fold(adjoint, "lat", h, 1, False)
    gradient = fold(adjoint, "lon", h, 2, True)
    cost = total(local_cost, ("lon", "lat"))
    return (gradient, cost)


def solution(mesh):
    placed = (
        P(None, "lat", "lon"),
        P(None, "lat", "lon"),
        P(None, "lat", "lon"),
        P(None, "lat", "lon"),
        P(None, "lat", "lon"),
        P(),
        P("lat", "lon", None, None),
        P("lat", "lon", None, None),
        P("lat", "lon", None, None),
        P("lat", "lon", None, None),
    )
    return jax.shard_map(
        on_device,
        mesh=mesh,
        in_specs=placed,
        out_specs=(P(None, "lat", "lon"), P()),
        check_vma=False,
    )
```

```python
import jax
import jax.numpy as jnp
from jax import lax
from jax.sharding import PartitionSpec as P

STEPS = 4
HALO = STEPS


def face_parts(velocity, branch):
    share = jnp.where(branch == 1, jnp.where(velocity > 0, 1.0, 0.0), 0.5)
    return (velocity * share, velocity * (1.0 - share))


def vertical(field, mixing):
    flux = mixing[:, None, None] * (field[1:] - field[:-1])
    zero_row = jnp.zeros_like(field[:1])
    return jnp.concatenate([flux, zero_row], 0) - jnp.concatenate([zero_row, flux], 0)


def shift(x, offset, dim):
    pad = [(0, 0)] * x.ndim
    size = x.shape[dim]
    if offset > 0:
        pad[dim] = (offset, 0)
        return lax.slice_in_dim(jnp.pad(x, pad), 0, size, axis=dim)
    pad[dim] = (0, -offset)
    return lax.slice_in_dim(jnp.pad(x, pad), -offset, size - offset, axis=dim)


def send(x, axis, pairs):
    return lax.ppermute(x.reshape(-1), axis, pairs).reshape(x.shape)


def ring(axis, periodic):
    count = lax.axis_size(axis)
    up = [(i, i + 1) for i in range(count - 1)]
    if periodic:
        up.append((count - 1, 0))
    down = [(t, s) for s, t in up]
    return up, down


def grow(block, axis, width, dim, periodic):
    up, down = ring(axis, periodic)
    size = block.shape[dim]
    low = send(lax.slice_in_dim(block, size - width, size, axis=dim), axis, up)
    high = send(lax.slice_in_dim(block, 0, width, axis=dim), axis, down)
    return jnp.concatenate([low, block, high], axis=dim)


def fold(block, axis, width, dim, periodic):
    up, down = ring(axis, periodic)
    size = block.shape[dim]
    from_high = send(lax.slice_in_dim(block, size - width, size, axis=dim), axis, up)
    from_low = send(lax.slice_in_dim(block, 0, width, axis=dim), axis, down)
    inner = lax.slice_in_dim(block, width, size - width, axis=dim)
    n = inner.shape[dim]
    pad_lo = [(0, 0)] * block.ndim
    pad_hi = [(0, 0)] * block.ndim
    pad_lo[dim] = (0, n - width)
    pad_hi[dim] = (n - width, 0)
    return inner + jnp.pad(from_high, pad_lo) + jnp.pad(from_low, pad_hi)


def total(value, axes):
    for axis in axes:
        count = lax.axis_size(axis)
        step = 1
        while step < count:
            pairs = [(i, i ^ step) for i in range(count)]
            value = value + lax.ppermute(value, axis, pairs)
            step *= 2
    return value


def on_device(
    initial,
    east_wind,
    north_wind,
    east_mask,
    north_mask,
    mixing,
    obs_cell,
    obs_level,
    obs_value,
    obs_weight,
):
    levels, rows, cols = initial.shape
    h = HALO
    west_p, west_q = face_parts(east_wind, east_mask)
    south_p, south_q = face_parts(north_wind, north_mask)
    global_row = lax.axis_index("lat") * rows + lax.iota(jnp.int32, rows)
    keep = (global_row > 0)[None, :, None]
    south_p = jnp.where(keep, south_p, 0.0)
    south_q = jnp.where(keep, south_q, 0.0)

    fields = jnp.stack([initial, west_p, west_q, south_p, south_q])
    fields = grow(fields, "lon", h, 3, True)
    fields = grow(fields, "lat", h, 2, False)

    state = fields[0]
    px, qx, py, qy = fields[1], fields[2], fields[3], fields[4]
    pxe = shift(px, -1, 2)
    qxe = shift(qx, -1, 2)
    pyn = shift(py, -1, 1)
    qyn = shift(qy, -1, 1)
    centre = (pxe - qx) + (pyn - qy)

    def forward_step(x):
        west = shift(x, 1, 2)
        east = shift(x, -1, 2)
        south = shift(x, 1, 1)
        north = shift(x, -1, 1)
        flow = centre * x + qxe * east - px * west + qyn * north - py * south
        return x + vertical(x, mixing) - flow

    def reverse_step(a):
        west = shift(a, 1, 2)
        east = shift(a, -1, 2)
        south = shift(a, 1, 1)
        north = shift(a, -1, 1)
        back = -centre * a - qx * west + pxe * east - qy * south + pyn * north
        return a + vertical(a, mixing) + back

    flat = obs_level[0, 0] * (rows * cols) + obs_cell[0, 0]
    local_cost = jnp.zeros((), jnp.float32)
    injections = []
    for step in range(STEPS):
        state = forward_step(state)
        inner = state[:, h : h + rows, h : h + cols]
        innovation = inner.reshape(-1)[flat[step]] - obs_value[0, 0, step]
        weighted = obs_weight[0, 0, step] * innovation
        local_cost = local_cost + 0.5 * jnp.sum(weighted * innovation)
        injected = jnp.zeros((levels * rows * cols,), jnp.float32).at[flat[step]].add(weighted)
        injections.append(jnp.pad(injected.reshape(levels, rows, cols), ((0, 0), (h, h), (h, h))))
    adjoint = jnp.zeros_like(injections[0])
    for step in range(STEPS - 1, -1, -1):
        adjoint = reverse_step(adjoint + injections[step])
    adjoint = fold(adjoint, "lat", h, 1, False)
    gradient = fold(adjoint, "lon", h, 2, True)
    cost = total(local_cost, ("lon", "lat"))
    return (gradient, cost)


def solution(mesh):
    placed = (
        P(None, "lat", "lon"),
        P(None, "lat", "lon"),
        P(None, "lat", "lon"),
        P(None, "lat", "lon"),
        P(None, "lat", "lon"),
        P(),
        P("lat", "lon", None, None),
        P("lat", "lon", None, None),
        P("lat", "lon", None, None),
        P("lat", "lon", None, None),
    )
    return jax.shard_map(
        on_device,
        mesh=mesh,
        in_specs=placed,
        out_specs=(P(None, "lat", "lon"), P()),
        check_vma=False,
    )
```

```python
import jax
import jax.numpy as jnp
from jax import lax
from jax.sharding import PartitionSpec as P

STEPS = 4
HALO = STEPS


def face_parts(velocity, branch):
    share = jnp.where(branch == 1, jnp.where(velocity > 0, 1.0, 0.0), 0.5)
    return (velocity * share, velocity * (1.0 - share))


def vertical(field, mixing):
    flux = mixing[:, None, None] * (field[1:] - field[:-1])
    zero_row = jnp.zeros_like(field[:1])
    return jnp.concatenate([flux, zero_row], 0) - jnp.concatenate([zero_row, flux], 0)


def shift(x, offset, dim):
    pad = [(0, 0)] * x.ndim
    size = x.shape[dim]
    if offset > 0:
        pad[dim] = (offset, 0)
        return lax.slice_in_dim(jnp.pad(x, pad), 0, size, axis=dim)
    pad[dim] = (0, -offset)
    return lax.slice_in_dim(jnp.pad(x, pad), -offset, size - offset, axis=dim)


def ring(axis, periodic):
    count = lax.axis_size(axis)
    up = [(i, i + 1) for i in range(count - 1)]
    if periodic:
        up.append((count - 1, 0))
    down = [(t, s) for s, t in up]
    return up, down


def grow(block, axis, width, dim, periodic):
    up, down = ring(axis, periodic)
    size = block.shape[dim]
    low = lax.ppermute(lax.slice_in_dim(block, size - width, size, axis=dim), axis, up)
    high = lax.ppermute(lax.slice_in_dim(block, 0, width, axis=dim), axis, down)
    return jnp.concatenate([low, block, high], axis=dim)


def fold(block, axis, width, dim, periodic):
    up, down = ring(axis, periodic)
    size = block.shape[dim]
    from_high = lax.ppermute(lax.slice_in_dim(block, size - width, size, axis=dim), axis, up)
    from_low = lax.ppermute(lax.slice_in_dim(block, 0, width, axis=dim), axis, down)
    inner = lax.slice_in_dim(block, width, size - width, axis=dim)
    n = inner.shape[dim]
    pad_lo = [(0, 0)] * block.ndim
    pad_hi = [(0, 0)] * block.ndim
    pad_lo[dim] = (0, n - width)
    pad_hi[dim] = (n - width, 0)
    return inner + jnp.pad(from_high, pad_lo) + jnp.pad(from_low, pad_hi)


def total(value, axes):
    for axis in axes:
        count = lax.axis_size(axis)
        step = 1
        while step < count:
            pairs = [(i, i ^ step) for i in range(count)]
            value = value + lax.ppermute(value, axis, pairs)
            step *= 2
    return value


def on_device(
    initial,
    east_wind,
    north_wind,
    east_mask,
    north_mask,
    mixing,
    obs_cell,
    obs_level,
    obs_value,
    obs_weight,
):
    levels, rows, cols = initial.shape
    h = HALO
    west_p, west_q = face_parts(east_wind, east_mask)
    south_p, south_q = face_parts(north_wind, north_mask)
    global_row = lax.axis_index("lat") * rows + lax.iota(jnp.int32, rows)
    keep = (global_row > 0)[None, :, None]
    south_p = jnp.where(keep, south_p, 0.0)
    south_q = jnp.where(keep, south_q, 0.0)

    fields = jnp.stack([initial, west_p, west_q, south_p, south_q])
    fields = grow(fields, "lon", h, 3, True)
    fields = grow(fields, "lat", h, 2, False)

    state = fields[0]
    px, qx, py, qy = fields[1], fields[2], fields[3], fields[4]
    pxe = shift(px, -1, 2)
    qxe = shift(qx, -1, 2)
    pyn = shift(py, -1, 1)
    qyn = shift(qy, -1, 1)
    centre = (pxe - qx) + (pyn - qy)

    def forward_step(x):
        west = shift(x, 1, 2)
        east = shift(x, -1, 2)
        south = shift(x, 1, 1)
        north = shift(x, -1, 1)
        flow = centre * x + qxe * east - px * west + qyn * north - py * south
        return x + vertical(x, mixing) - flow

    def reverse_step(a):
        west = shift(a, 1, 2)
        east = shift(a, -1, 2)
        south = shift(a, 1, 1)
        north = shift(a, -1, 1)
        back = -centre * a - qx * west + pxe * east - qy * south + pyn * north
        return a + vertical(a, mixing) + back

    flat = obs_level[0, 0] * (rows * cols) + obs_cell[0, 0]
    level = obs_level[0, 0]
    row = obs_cell[0, 0] // cols + h
    col = obs_cell[0, 0] % cols + h
    local_cost = jnp.zeros((), jnp.float32)
    injections = []
    for step in range(STEPS):
        state = forward_step(state)
        inner = state[:, h : h + rows, h : h + cols]
        innovation = inner.reshape(-1)[flat[step]] - obs_value[0, 0, step]
        weighted = obs_weight[0, 0, step] * innovation
        local_cost = local_cost + 0.5 * jnp.sum(weighted * innovation)
        injections.append(
            jnp.zeros((levels, rows + 2 * h, cols + 2 * h), jnp.float32)
            .at[level[step], row[step], col[step]]
            .add(weighted)
        )
    adjoint = jnp.zeros_like(injections[0])
    for step in range(STEPS - 1, -1, -1):
        adjoint = reverse_step(adjoint + injections[step])
    adjoint = fold(adjoint, "lat", h, 1, False)
    gradient = fold(adjoint, "lon", h, 2, True)
    cost = total(local_cost, ("lon", "lat"))
    return (gradient, cost)


def solution(mesh):
    placed = (
        P(None, "lat", "lon"),
        P(None, "lat", "lon"),
        P(None, "lat", "lon"),
        P(None, "lat", "lon"),
        P(None, "lat", "lon"),
        P(),
        P("lat", "lon", None, None),
        P("lat", "lon", None, None),
        P("lat", "lon", None, None),
        P("lat", "lon", None, None),
    )
    return jax.shard_map(
        on_device,
        mesh=mesh,
        in_specs=placed,
        out_specs=(P(None, "lat", "lon"), P()),
        check_vma=False,
    )
```

```python
import jax
import jax.numpy as jnp
from jax import lax
from jax.sharding import PartitionSpec as P

STEPS = 4
HALO = STEPS


def face_parts(velocity, branch):
    share = jnp.where(branch == 1, jnp.where(velocity > 0, 1.0, 0.0), 0.5)
    return (velocity * share, velocity * (1.0 - share))


def vertical(field, mixing):
    flux = mixing[:, None, None] * (field[1:] - field[:-1])
    zero_row = jnp.zeros_like(field[:1])
    return jnp.concatenate([flux, zero_row], 0) - jnp.concatenate([zero_row, flux], 0)


def shift(x, offset, dim):
    pad = [(0, 0)] * x.ndim
    size = x.shape[dim]
    if offset > 0:
        pad[dim] = (offset, 0)
        return lax.slice_in_dim(jnp.pad(x, pad), 0, size, axis=dim)
    pad[dim] = (0, -offset)
    return lax.slice_in_dim(jnp.pad(x, pad), -offset, size - offset, axis=dim)


def ring(axis, periodic):
    count = lax.axis_size(axis)
    up = [(i, i + 1) for i in range(count - 1)]
    if periodic:
        up.append((count - 1, 0))
    down = [(t, s) for s, t in up]
    return up, down


def grow(block, axis, width, dim, periodic):
    up, down = ring(axis, periodic)
    size = block.shape[dim]
    low = lax.ppermute(lax.slice_in_dim(block, size - width, size, axis=dim), axis, up)
    high = lax.ppermute(lax.slice_in_dim(block, 0, width, axis=dim), axis, down)
    return jnp.concatenate([low, block, high], axis=dim)


def fold(block, axis, width, dim, periodic, value):
    up, down = ring(axis, periodic)
    size = block.shape[dim]
    slab = jnp.broadcast_to(value, (1,) + tuple(n if d != dim else width for d, n in enumerate(block.shape[1:], 1)))
    top = jnp.concatenate([lax.slice_in_dim(block, size - width, size, axis=dim), slab], 0)
    bottom = jnp.concatenate([lax.slice_in_dim(block, 0, width, axis=dim), slab], 0)
    from_high = lax.ppermute(top, axis, up)
    from_low = lax.ppermute(bottom, axis, down)
    levels = block.shape[0]
    odd = lax.axis_index(axis) % 2 == 1
    partner = jnp.where(odd, from_high[levels].reshape(-1)[0], from_low[levels].reshape(-1)[0])
    from_high = from_high[:levels]
    from_low = from_low[:levels]
    inner = lax.slice_in_dim(block, width, size - width, axis=dim)
    n = inner.shape[dim]
    pad_lo = [(0, 0)] * block.ndim
    pad_hi = [(0, 0)] * block.ndim
    pad_lo[dim] = (0, n - width)
    pad_hi[dim] = (n - width, 0)
    return inner + jnp.pad(from_high, pad_lo) + jnp.pad(from_low, pad_hi), value + partner


def total(value, axes, first):
    for axis in axes:
        count = lax.axis_size(axis)
        step = first
        while step < count:
            pairs = [(i, i ^ step) for i in range(count)]
            value = value + lax.ppermute(value, axis, pairs)
            step *= 2
    return value


def on_device(
    initial,
    east_wind,
    north_wind,
    east_mask,
    north_mask,
    mixing,
    obs_cell,
    obs_level,
    obs_value,
    obs_weight,
):
    levels, rows, cols = initial.shape
    h = HALO
    west_p, west_q = face_parts(east_wind, east_mask)
    south_p, south_q = face_parts(north_wind, north_mask)
    global_row = lax.axis_index("lat") * rows + lax.iota(jnp.int32, rows)
    keep = (global_row > 0)[None, :, None]
    south_p = jnp.where(keep, south_p, 0.0)
    south_q = jnp.where(keep, south_q, 0.0)

    fields = jnp.stack([initial, west_p, west_q, south_p, south_q])
    fields = grow(fields, "lon", h, 3, True)
    fields = grow(fields, "lat", h, 2, False)

    state = fields[0]
    px, qx, py, qy = fields[1], fields[2], fields[3], fields[4]
    pxe = shift(px, -1, 2)
    qxe = shift(qx, -1, 2)
    pyn = shift(py, -1, 1)
    qyn = shift(qy, -1, 1)
    centre = (pxe - qx) + (pyn - qy)

    def forward_step(x):
        west = shift(x, 1, 2)
        east = shift(x, -1, 2)
        south = shift(x, 1, 1)
        north = shift(x, -1, 1)
        flow = centre * x + qxe * east - px * west + qyn * north - py * south
        return x + vertical(x, mixing) - flow

    def reverse_step(a):
        west = shift(a, 1, 2)
        east = shift(a, -1, 2)
        south = shift(a, 1, 1)
        north = shift(a, -1, 1)
        back = -centre * a - qx * west + pxe * east - qy * south + pyn * north
        return a + vertical(a, mixing) + back

    flat = obs_level[0, 0] * (rows * cols) + obs_cell[0, 0]
    local_cost = jnp.zeros((), jnp.float32)
    injections = []
    for step in range(STEPS):
        state = forward_step(state)
        inner = state[:, h : h + rows, h : h + cols]
        innovation = inner.reshape(-1)[flat[step]] - obs_value[0, 0, step]
        weighted = obs_weight[0, 0, step] * innovation
        local_cost = local_cost + 0.5 * jnp.sum(weighted * innovation)
        injected = jnp.zeros((levels * rows * cols,), jnp.float32).at[flat[step]].add(weighted)
        injections.append(jnp.pad(injected.reshape(levels, rows, cols), ((0, 0), (h, h), (h, h))))
    adjoint = jnp.zeros_like(injections[0])
    for step in range(STEPS - 1, -1, -1):
        adjoint = reverse_step(adjoint + injections[step])
    adjoint, value = fold(adjoint, "lat", h, 1, False, local_cost)
    gradient, value = fold(adjoint, "lon", h, 2, True, value)
    cost = total(value, ("lon", "lat"), 2)
    return (gradient, cost)


def solution(mesh):
    placed = (
        P(None, "lat", "lon"),
        P(None, "lat", "lon"),
        P(None, "lat", "lon"),
        P(None, "lat", "lon"),
        P(None, "lat", "lon"),
        P(),
        P("lat", "lon", None, None),
        P("lat", "lon", None, None),
        P("lat", "lon", None, None),
        P("lat", "lon", None, None),
    )
    return jax.shard_map(
        on_device,
        mesh=mesh,
        in_specs=placed,
        out_specs=(P(None, "lat", "lon"), P()),
        check_vma=False,
    )
```

```python
import jax
import jax.numpy as jnp
from jax import lax
from jax.sharding import PartitionSpec as P

STEPS = 4
HALO = STEPS


def face_parts(velocity, branch):
    share = jnp.where(branch == 1, jnp.where(velocity > 0, 1.0, 0.0), 0.5)
    return (velocity * share, velocity * (1.0 - share))


def vertical(field, mixing):
    flux = mixing[:, None, None] * (field[1:] - field[:-1])
    zero_row = jnp.zeros_like(field[:1])
    return jnp.concatenate([flux, zero_row], 0) - jnp.concatenate([zero_row, flux], 0)


def shift(x, offset, dim):
    pad = [(0, 0)] * x.ndim
    size = x.shape[dim]
    if offset > 0:
        pad[dim] = (offset, 0)
        return lax.slice_in_dim(jnp.pad(x, pad), 0, size, axis=dim)
    pad[dim] = (0, -offset)
    return lax.slice_in_dim(jnp.pad(x, pad), -offset, size - offset, axis=dim)


def ring(axis, periodic):
    count = lax.axis_size(axis)
    up = [(i, i + 1) for i in range(count - 1)]
    if periodic:
        up.append((count - 1, 0))
    down = [(t, s) for s, t in up]
    return up, down


def grow(block, axis, width, dim, periodic):
    up, down = ring(axis, periodic)
    size = block.shape[dim]
    low = lax.ppermute(lax.slice_in_dim(block, size - width, size, axis=dim), axis, up)
    high = lax.ppermute(lax.slice_in_dim(block, 0, width, axis=dim), axis, down)
    return jnp.concatenate([low, block, high], axis=dim)


def fold(block, axis, width, dim, periodic, value):
    up, down = ring(axis, periodic)
    size = block.shape[dim]
    slab = jnp.broadcast_to(value, (1,) + tuple(n if d != dim else width for d, n in enumerate(block.shape[1:], 1)))
    top = jnp.concatenate([lax.slice_in_dim(block, size - width, size, axis=dim), slab], 0)
    bottom = jnp.concatenate([lax.slice_in_dim(block, 0, width, axis=dim), slab], 0)
    from_high = lax.ppermute(top, axis, up)
    from_low = lax.ppermute(bottom, axis, down)
    levels = block.shape[0]
    odd = lax.axis_index(axis) % 2 == 1
    partner = jnp.where(odd, from_high[levels].reshape(-1)[0], from_low[levels].reshape(-1)[0])
    from_high = from_high[:levels]
    from_low = from_low[:levels]
    inner = lax.slice_in_dim(block, width, size - width, axis=dim)
    n = inner.shape[dim]
    pad_lo = [(0, 0)] * block.ndim
    pad_hi = [(0, 0)] * block.ndim
    pad_lo[dim] = (0, n - width)
    pad_hi[dim] = (n - width, 0)
    return inner + jnp.pad(from_high, pad_lo) + jnp.pad(from_low, pad_hi), value + partner


def total(value, axes, first):
    for axis in axes:
        count = lax.axis_size(axis)
        step = first
        while step < count:
            pairs = [(i, i ^ step) for i in range(count)]
            value = value + lax.ppermute(value, axis, pairs)
            step *= 2
    return value


def on_device(
    initial,
    east_wind,
    north_wind,
    east_mask,
    north_mask,
    mixing,
    obs_cell,
    obs_level,
    obs_value,
    obs_weight,
):
    levels, rows, cols = initial.shape
    h = HALO
    west_p, west_q = face_parts(east_wind, east_mask)
    south_p, south_q = face_parts(north_wind, north_mask)
    global_row = lax.axis_index("lat") * rows + lax.iota(jnp.int32, rows)
    keep = (global_row > 0)[None, :, None]
    south_p = jnp.where(keep, south_p, 0.0)
    south_q = jnp.where(keep, south_q, 0.0)

    fields = jnp.stack([initial, west_p, west_q, south_p, south_q])
    fields = grow(fields, "lat", h, 2, False)
    fields = grow(fields, "lon", h, 3, True)

    state = fields[0]
    px, qx, py, qy = fields[1], fields[2], fields[3], fields[4]
    pxe = shift(px, -1, 2)
    qxe = shift(qx, -1, 2)
    pyn = shift(py, -1, 1)
    qyn = shift(qy, -1, 1)
    centre = (pxe - qx) + (pyn - qy)

    def forward_step(x):
        west = shift(x, 1, 2)
        east = shift(x, -1, 2)
        south = shift(x, 1, 1)
        north = shift(x, -1, 1)
        flow = centre * x + qxe * east - px * west + qyn * north - py * south
        return x + vertical(x, mixing) - flow

    def reverse_step(a):
        west = shift(a, 1, 2)
        east = shift(a, -1, 2)
        south = shift(a, 1, 1)
        north = shift(a, -1, 1)
        back = -centre * a - qx * west + pxe * east - qy * south + pyn * north
        return a + vertical(a, mixing) + back

    flat = obs_level[0, 0] * (rows * cols) + obs_cell[0, 0]
    local_cost = jnp.zeros((), jnp.float32)
    injections = []
    for step in range(STEPS):
        state = forward_step(state)
        inner = state[:, h : h + rows, h : h + cols]
        innovation = inner.reshape(-1)[flat[step]] - obs_value[0, 0, step]
        weighted = obs_weight[0, 0, step] * innovation
        local_cost = local_cost + 0.5 * jnp.sum(weighted * innovation)
        injected = jnp.zeros((levels * rows * cols,), jnp.float32).at[flat[step]].add(weighted)
        injections.append(jnp.pad(injected.reshape(levels, rows, cols), ((0, 0), (h, h), (h, h))))
    adjoint = jnp.zeros_like(injections[0])
    for step in range(STEPS - 1, -1, -1):
        adjoint = reverse_step(adjoint + injections[step])
    adjoint, value = fold(adjoint, "lon", h, 2, True, local_cost)
    gradient, value = fold(adjoint, "lat", h, 1, False, value)
    cost = total(value, ("lon", "lat"), 2)
    return (gradient, cost)


def solution(mesh):
    placed = (
        P(None, "lat", "lon"),
        P(None, "lat", "lon"),
        P(None, "lat", "lon"),
        P(None, "lat", "lon"),
        P(None, "lat", "lon"),
        P(),
        P("lat", "lon", None, None),
        P("lat", "lon", None, None),
        P("lat", "lon", None, None),
        P("lat", "lon", None, None),
    )
    return jax.shard_map(
        on_device,
        mesh=mesh,
        in_specs=placed,
        out_specs=(P(None, "lat", "lon"), P()),
        check_vma=False,
    )
```

```python
import jax
import jax.numpy as jnp
from jax import lax
from jax.sharding import PartitionSpec as P

STEPS = 4
HALO = STEPS


def face_parts(velocity, branch):
    share = jnp.where(branch == 1, jnp.where(velocity > 0, 1.0, 0.0), 0.5)
    return (velocity * share, velocity * (1.0 - share))


def vertical(field, mixing):
    flux = mixing[:, None, None] * (field[1:] - field[:-1])
    zero_row = jnp.zeros_like(field[:1])
    return jnp.concatenate([flux, zero_row], 0) - jnp.concatenate([zero_row, flux], 0)


def shift(x, offset, dim):
    pad = [(0, 0)] * x.ndim
    size = x.shape[dim]
    if offset > 0:
        pad[dim] = (offset, 0)
        return lax.slice_in_dim(jnp.pad(x, pad), 0, size, axis=dim)
    pad[dim] = (0, -offset)
    return lax.slice_in_dim(jnp.pad(x, pad), -offset, size - offset, axis=dim)


def ring(axis, periodic):
    count = lax.axis_size(axis)
    up = [(i, i + 1) for i in range(count - 1)]
    if periodic:
        up.append((count - 1, 0))
    down = [(t, s) for s, t in up]
    return up, down


def grow(block, axis, width, dim, periodic):
    up, down = ring(axis, periodic)
    size = block.shape[dim]
    low = lax.ppermute(lax.slice_in_dim(block, size - width, size, axis=dim), axis, up)
    high = lax.ppermute(lax.slice_in_dim(block, 0, width, axis=dim), axis, down)
    return jnp.concatenate([low, block, high], axis=dim)


def fold(block, axis, width, dim, periodic, value):
    up, down = ring(axis, periodic)
    size = block.shape[dim]
    slab = jnp.broadcast_to(value, (1,) + tuple(n if d != dim else width for d, n in enumerate(block.shape[1:], 1)))
    top = jnp.concatenate([lax.slice_in_dim(block, size - width, size, axis=dim), slab], 0)
    bottom = jnp.concatenate([lax.slice_in_dim(block, 0, width, axis=dim), slab], 0)
    from_high = lax.ppermute(top, axis, up)
    from_low = lax.ppermute(bottom, axis, down)
    levels = block.shape[0]
    odd = lax.axis_index(axis) % 2 == 1
    partner = jnp.where(odd, from_high[levels].reshape(-1)[0], from_low[levels].reshape(-1)[0])
    from_high = from_high[:levels]
    from_low = from_low[:levels]
    inner = lax.slice_in_dim(block, width, size - width, axis=dim)
    n = inner.shape[dim]
    pad_lo = [(0, 0)] * block.ndim
    pad_hi = [(0, 0)] * block.ndim
    pad_lo[dim] = (0, n - width)
    pad_hi[dim] = (n - width, 0)
    return inner + jnp.pad(from_high, pad_lo) + jnp.pad(from_low, pad_hi), value + partner


def total(value, axes, first):
    for axis in axes:
        count = lax.axis_size(axis)
        step = first
        while step < count:
            pairs = [(i, i ^ step) for i in range(count)]
            value = value + lax.ppermute(value, axis, pairs)
            step *= 2
    return value


def on_device(
    initial,
    east_wind,
    north_wind,
    east_mask,
    north_mask,
    mixing,
    obs_cell,
    obs_level,
    obs_value,
    obs_weight,
):
    levels, rows, cols = initial.shape
    h = HALO
    west_p, west_q = face_parts(east_wind, east_mask)
    south_p, south_q = face_parts(north_wind, north_mask)
    global_row = lax.axis_index("lat") * rows + lax.iota(jnp.int32, rows)
    keep = (global_row > 0)[None, :, None]
    south_p = jnp.where(keep, south_p, 0.0)
    south_q = jnp.where(keep, south_q, 0.0)

    fields = jnp.stack([initial, west_p, west_q, south_p, south_q])
    fields = grow(fields, "lat", h, 2, False)
    fields = grow(fields, "lon", h, 3, True)

    state = fields[0]
    px, qx, py, qy = fields[1], fields[2], fields[3], fields[4]
    pxe = shift(px, -1, 2)
    qxe = shift(qx, -1, 2)
    pyn = shift(py, -1, 1)
    qyn = shift(qy, -1, 1)
    centre = (pxe - qx) + (pyn - qy)

    def forward_step(x):
        west = shift(x, 1, 2)
        east = shift(x, -1, 2)
        south = shift(x, 1, 1)
        north = shift(x, -1, 1)
        flow = centre * x + qxe * east - px * west + qyn * north - py * south
        return x + vertical(x, mixing) - flow

    def reverse_step(a):
        west = shift(a, 1, 2)
        east = shift(a, -1, 2)
        south = shift(a, 1, 1)
        north = shift(a, -1, 1)
        back = -centre * a - qx * west + pxe * east - qy * south + pyn * north
        return a + vertical(a, mixing) + back

    flat = obs_level[0, 0] * (rows * cols) + obs_cell[0, 0]
    local_cost = jnp.zeros((), jnp.float32)
    injections = []
    for step in range(STEPS):
        state = forward_step(state)
        inner = state[:, h : h + rows, h : h + cols]
        innovation = inner.reshape(-1)[flat[step]] - obs_value[0, 0, step]
        weighted = obs_weight[0, 0, step] * innovation
        local_cost = local_cost + 0.5 * jnp.sum(weighted * innovation)
        injections.append(weighted)
    block = levels * rows * cols
    spots = jnp.arange(STEPS, dtype=jnp.int32)[:, None] * block + flat
    injected = jnp.zeros((STEPS * block,), jnp.float32).at[spots].add(jnp.stack(injections))
    injected = injected.reshape(STEPS, levels, rows, cols)
    injections = [jnp.pad(injected[k], ((0, 0), (h, h), (h, h))) for k in range(STEPS)]
    adjoint = jnp.zeros_like(injections[0])
    for step in range(STEPS - 1, -1, -1):
        adjoint = reverse_step(adjoint + injections[step])
    adjoint, value = fold(adjoint, "lon", h, 2, True, local_cost)
    gradient, value = fold(adjoint, "lat", h, 1, False, value)
    cost = total(value, ("lon", "lat"), 2)
    return (gradient, cost)


def solution(mesh):
    placed = (
        P(None, "lat", "lon"),
        P(None, "lat", "lon"),
        P(None, "lat", "lon"),
        P(None, "lat", "lon"),
        P(None, "lat", "lon"),
        P(),
        P("lat", "lon", None, None),
        P("lat", "lon", None, None),
        P("lat", "lon", None, None),
        P("lat", "lon", None, None),
    )
    return jax.shard_map(
        on_device,
        mesh=mesh,
        in_specs=placed,
        out_specs=(P(None, "lat", "lon"), P()),
        check_vma=False,
    )
```

```python
import jax
import jax.numpy as jnp
from jax import lax
from jax.sharding import PartitionSpec as P

STEPS = 4
HALO = STEPS


def face_parts(velocity, branch):
    share = jnp.where(branch == 1, jnp.where(velocity > 0, 1.0, 0.0), 0.5)
    return (velocity * share, velocity * (1.0 - share))


def vertical(field, mixing):
    flux = mixing[:, None, None] * (field[1:] - field[:-1])
    zero_row = jnp.zeros_like(field[:1])
    return jnp.concatenate([flux, zero_row], 0) - jnp.concatenate([zero_row, flux], 0)


def shift(x, offset, dim):
    pad = [(0, 0)] * x.ndim
    size = x.shape[dim]
    if offset > 0:
        pad[dim] = (offset, 0)
        return lax.slice_in_dim(jnp.pad(x, pad), 0, size, axis=dim)
    pad[dim] = (0, -offset)
    return lax.slice_in_dim(jnp.pad(x, pad), -offset, size - offset, axis=dim)


def ring(axis, periodic):
    count = lax.axis_size(axis)
    up = [(i, i + 1) for i in range(count - 1)]
    if periodic:
        up.append((count - 1, 0))
    down = [(t, s) for s, t in up]
    return up, down


def grow(block, axis, width, dim, periodic):
    up, down = ring(axis, periodic)
    size = block.shape[dim]
    low = lax.ppermute(lax.slice_in_dim(block, size - width, size, axis=dim), axis, up)
    high = lax.ppermute(lax.slice_in_dim(block, 0, width, axis=dim), axis, down)
    return jnp.concatenate([low, block, high], axis=dim)


def fold(block, axis, width, dim, periodic, value):
    up, down = ring(axis, periodic)
    size = block.shape[dim]
    slab = jnp.broadcast_to(value, (1,) + tuple(n if d != dim else width for d, n in enumerate(block.shape[1:], 1)))
    top = jnp.concatenate([lax.slice_in_dim(block, size - width, size, axis=dim), slab], 0)
    bottom = jnp.concatenate([lax.slice_in_dim(block, 0, width, axis=dim), slab], 0)
    from_high = lax.ppermute(top, axis, up)
    from_low = lax.ppermute(bottom, axis, down)
    levels = block.shape[0]
    odd = lax.axis_index(axis) % 2 == 1
    partner = jnp.where(odd, from_high[levels].reshape(-1)[0], from_low[levels].reshape(-1)[0])
    from_high = from_high[:levels]
    from_low = from_low[:levels]
    inner = lax.slice_in_dim(block, width, size - width, axis=dim)
    n = inner.shape[dim]
    pad_lo = [(0, 0)] * block.ndim
    pad_hi = [(0, 0)] * block.ndim
    pad_lo[dim] = (0, n - width)
    pad_hi[dim] = (n - width, 0)
    return inner + jnp.pad(from_high, pad_lo) + jnp.pad(from_low, pad_hi), value + partner


def total(value, axes, first):
    for axis in axes:
        count = lax.axis_size(axis)
        step = first
        while step < count:
            pairs = [(i, i ^ step) for i in range(count)]
            value = value + lax.ppermute(value, axis, pairs)
            step *= 2
    return value


def on_device(
    initial,
    east_wind,
    north_wind,
    east_mask,
    north_mask,
    mixing,
    obs_cell,
    obs_level,
    obs_value,
    obs_weight,
):
    levels, rows, cols = initial.shape
    h = HALO
    west_p, west_q = face_parts(east_wind, east_mask)
    south_p, south_q = face_parts(north_wind, north_mask)
    global_row = lax.axis_index("lat") * rows + lax.iota(jnp.int32, rows)
    keep = (global_row > 0)[None, :, None]
    south_p = jnp.where(keep, south_p, 0.0)
    south_q = jnp.where(keep, south_q, 0.0)

    fields = jnp.stack([initial, west_p, west_q, south_p, south_q])
    fields = grow(fields, "lat", h, 2, False)
    fields = grow(fields, "lon", h, 3, True)

    state = fields[0]
    px, qx, py, qy = fields[1], fields[2], fields[3], fields[4]
    pxe = shift(px, -1, 2)
    qxe = shift(qx, -1, 2)
    pyn = shift(py, -1, 1)
    qyn = shift(qy, -1, 1)
    centre = (pxe - qx) + (pyn - qy)

    def forward_step(x):
        west = shift(x, 1, 2)
        east = shift(x, -1, 2)
        south = shift(x, 1, 1)
        north = shift(x, -1, 1)
        flow = centre * x + qxe * east - px * west + qyn * north - py * south
        return x + vertical(x, mixing) - flow

    def reverse_step(a):
        west = shift(a, 1, 2)
        east = shift(a, -1, 2)
        south = shift(a, 1, 1)
        north = shift(a, -1, 1)
        back = -centre * a - qx * west + pxe * east - qy * south + pyn * north
        return a + vertical(a, mixing) + back

    flat = obs_level[0, 0] * (rows * cols) + obs_cell[0, 0]
    inner = []
    for step in range(STEPS):
        state = forward_step(state)
        inner.append(state[:, h : h + rows, h : h + cols])
    block = levels * rows * cols
    spots = jnp.arange(STEPS, dtype=jnp.int32)[:, None] * block + flat
    innovation = jnp.stack(inner).reshape(-1)[spots] - obs_value[0, 0]
    weighted = obs_weight[0, 0] * innovation
    local_cost = 0.5 * jnp.sum(weighted * innovation)
    injected = jnp.zeros((STEPS * block,), jnp.float32).at[spots].add(weighted)
    injected = injected.reshape(STEPS, levels, rows, cols)
    injections = [jnp.pad(injected[k], ((0, 0), (h, h), (h, h))) for k in range(STEPS)]
    adjoint = jnp.zeros_like(injections[0])
    for step in range(STEPS - 1, -1, -1):
        adjoint = reverse_step(adjoint + injections[step])
    adjoint, value = fold(adjoint, "lon", h, 2, True, local_cost)
    gradient, value = fold(adjoint, "lat", h, 1, False, value)
    cost = total(value, ("lon", "lat"), 2)
    return (gradient, cost)


def solution(mesh):
    placed = (
        P(None, "lat", "lon"),
        P(None, "lat", "lon"),
        P(None, "lat", "lon"),
        P(None, "lat", "lon"),
        P(None, "lat", "lon"),
        P(),
        P("lat", "lon", None, None),
        P("lat", "lon", None, None),
        P("lat", "lon", None, None),
        P("lat", "lon", None, None),
    )
    return jax.shard_map(
        on_device,
        mesh=mesh,
        in_specs=placed,
        out_specs=(P(None, "lat", "lon"), P()),
        check_vma=False,
    )
```

```python
import jax
import jax.numpy as jnp
from jax import lax
from jax.sharding import PartitionSpec as P

STEPS = 4
HALO = STEPS


def face_parts(velocity, branch):
    share = jnp.where(branch == 1, jnp.where(velocity > 0, 1.0, 0.0), 0.5)
    return (velocity * share, velocity * (1.0 - share))


def vertical(field, mixing):
    flux = mixing[:, None, None] * (field[1:] - field[:-1])
    zero_row = jnp.zeros_like(field[:1])
    return jnp.concatenate([flux, zero_row], 0) - jnp.concatenate([zero_row, flux], 0)


def shift(x, offset, dim):
    pad = [(0, 0)] * x.ndim
    size = x.shape[dim]
    if offset > 0:
        pad[dim] = (offset, 0)
        return lax.slice_in_dim(jnp.pad(x, pad), 0, size, axis=dim)
    pad[dim] = (0, -offset)
    return lax.slice_in_dim(jnp.pad(x, pad), -offset, size - offset, axis=dim)


def ring(axis, periodic):
    count = lax.axis_size(axis)
    up = [(i, i + 1) for i in range(count - 1)]
    if periodic:
        up.append((count - 1, 0))
    down = [(t, s) for s, t in up]
    return up, down


def grow(block, axis, width, dim, periodic):
    up, down = ring(axis, periodic)
    size = block.shape[dim]
    low = lax.ppermute(lax.slice_in_dim(block, size - width, size, axis=dim), axis, up)
    high = lax.ppermute(lax.slice_in_dim(block, 0, width, axis=dim), axis, down)
    return jnp.concatenate([low, block, high], axis=dim)


def fold(block, axis, width, dim, periodic, value):
    up, down = ring(axis, periodic)
    size = block.shape[dim]
    slab = jnp.broadcast_to(value, (1,) + tuple(n if d != dim else width for d, n in enumerate(block.shape[1:], 1)))
    top = jnp.concatenate([lax.slice_in_dim(block, size - width, size, axis=dim), slab], 0)
    bottom = jnp.concatenate([lax.slice_in_dim(block, 0, width, axis=dim), slab], 0)
    from_high = lax.ppermute(top, axis, up)
    from_low = lax.ppermute(bottom, axis, down)
    levels = block.shape[0]
    odd = lax.axis_index(axis) % 2 == 1
    partner = jnp.where(odd, from_high[levels].reshape(-1)[0], from_low[levels].reshape(-1)[0])
    from_high = from_high[:levels]
    from_low = from_low[:levels]
    inner = lax.slice_in_dim(block, width, size - width, axis=dim)
    n = inner.shape[dim]
    pad_lo = [(0, 0)] * block.ndim
    pad_hi = [(0, 0)] * block.ndim
    pad_lo[dim] = (0, n - width)
    pad_hi[dim] = (n - width, 0)
    return inner + jnp.pad(from_high, pad_lo) + jnp.pad(from_low, pad_hi), value + partner


def total(value, axes, first):
    for axis in axes:
        count = lax.axis_size(axis)
        step = first
        while step < count:
            pairs = [(i, i ^ step) for i in range(count)]
            value = value + lax.ppermute(value, axis, pairs)
            step *= 2
    return value


def on_device(
    initial,
    east_wind,
    north_wind,
    east_mask,
    north_mask,
    mixing,
    obs_cell,
    obs_level,
    obs_value,
    obs_weight,
):
    levels, rows, cols = initial.shape
    h = HALO
    west_p, west_q = face_parts(east_wind, east_mask)
    south_p, south_q = face_parts(north_wind, north_mask)
    global_row = lax.axis_index("lat") * rows + lax.iota(jnp.int32, rows)
    keep = (global_row > 0)[None, :, None]
    south_p = jnp.where(keep, south_p, 0.0)
    south_q = jnp.where(keep, south_q, 0.0)

    fields = jnp.stack([initial, west_p, west_q, south_p, south_q])
    fields = grow(fields, "lat", h, 2, False)
    fields = grow(fields, "lon", h, 3, True)

    state = fields[0]
    px, qx, py, qy = fields[1], fields[2], fields[3], fields[4]
    pxe = shift(px, -1, 2)
    qxe = shift(qx, -1, 2)
    pyn = shift(py, -1, 1)
    qyn = shift(qy, -1, 1)
    centre = (pxe - qx) + (pyn - qy)

    def forward_step(x):
        west = shift(x, 1, 2)
        east = shift(x, -1, 2)
        south = shift(x, 1, 1)
        north = shift(x, -1, 1)
        flow = centre * x + qxe * east - px * west + qyn * north - py * south
        return x + vertical(x, mixing) - flow

    def reverse_step(a):
        west = shift(a, 1, 2)
        east = shift(a, -1, 2)
        south = shift(a, 1, 1)
        north = shift(a, -1, 1)
        back = -centre * a - qx * west + pxe * east - qy * south + pyn * north
        return a + vertical(a, mixing) + back

    flat = obs_level[0, 0] * (rows * cols) + obs_cell[0, 0]
    inner = []
    for step in range(STEPS):
        state = forward_step(state)
        inner.append(state[:, h : h + rows, h : h + cols])
    block = levels * rows * cols
    spots = jnp.arange(STEPS, dtype=jnp.int32)[:, None] * block + flat
    innovation = jnp.stack(inner).reshape(-1)[spots] - obs_value[0, 0]
    weighted = obs_weight[0, 0] * innovation
    local_cost = 0.5 * jnp.sum(weighted * innovation)
    injected = jnp.zeros((STEPS * block,), jnp.float32).at[spots].add(weighted)
    injected = injected.reshape(STEPS, levels, rows, cols)
    padded = jnp.pad(injected, ((0, 0), (0, 0), (h, h), (h, h)))
    injections = [padded[k] for k in range(STEPS)]
    adjoint = jnp.zeros_like(injections[0])
    for step in range(STEPS - 1, -1, -1):
        adjoint = reverse_step(adjoint + injections[step])
    adjoint, value = fold(adjoint, "lon", h, 2, True, local_cost)
    gradient, value = fold(adjoint, "lat", h, 1, False, value)
    cost = total(value, ("lon", "lat"), 2)
    return (gradient, cost)


def solution(mesh):
    placed = (
        P(None, "lat", "lon"),
        P(None, "lat", "lon"),
        P(None, "lat", "lon"),
        P(None, "lat", "lon"),
        P(None, "lat", "lon"),
        P(),
        P("lat", "lon", None, None),
        P("lat", "lon", None, None),
        P("lat", "lon", None, None),
        P("lat", "lon", None, None),
    )
    return jax.shard_map(
        on_device,
        mesh=mesh,
        in_specs=placed,
        out_specs=(P(None, "lat", "lon"), P()),
        check_vma=False,
    )
```
